256 devices in a mesh: dp: 32 (over x, y, core), tensor: 8 (over z).
Axes of the slice: x: 4, y: 4, z: 8, core: 2. Of those that a mesh axis runs over, the one named last changes fastest.
Arguments:
- hidden_states: bfloat16 [24576, 4096], P('dp', 'tensor')
- neighbour_ids: int32 [384, 2], P('dp'), may hold values from 0 to 511, as said below
- database: bfloat16 [512, 128, 896], P('dp')
- w_up: bfloat16 [896, 3584], P(None, 'tensor'), may hold values from -0.1875 to 0.1875
- w_down: bfloat16 [3584, 896], P('tensor'), may hold values from -0.09375 to 0.09375
- w_query: bfloat16 [4096, 4096], P(None, 'tensor'), may hold values from -0.09375 to 0.09375
- w_key: bfloat16 [896, 4096], P(None, 'tensor'), may hold values from -0.1875 to 0.1875
- w_value: bfloat16 [896, 4096], P(None, 'tensor'), may hold values from -0.1875 to 0.1875
Outputs:
- attended: bfloat16 [24576, 4096], P('dp', 'tensor')
The draws below stay inside these ranges and needn't reach their ends.
Inputs may be any that keep to these rules, and one draw needn't show every extreme that they name: `neighbour_ids`: block ids are grouped by owner: index s of dp holds blocks s * 16 to (s + 1) * 16 - 1. Among the 24 ids of one sequence, no owner's blocks are named more than 2 times; one owner, the same for every sequence, is named exactly 2 times by each.
All inputs are finite; a program needn't handle non-finite values.
Results may differ from the reference program's by a relative error of at most 0.02.
Values may be sent and summed in bfloat16 or wider, within the bound.
No kernel may reach another device: no remote copies, remote signals or barrier semaphores. Data moves between devices by JAX's collectives and lax.ppermute only.
A program may use at most 128 MiB of HBM per device.

```python
import math
import jax
import jax.numpy as jnp
from jax import lax

D = 4096
HEADS = 32
HD = 128
E = 896
FF = 3584
SPAN = 64
KN = 2
NTOK = 128
CH = 12
DB_DEV = 16
SEQ = 768
TOKENS = 24576
SPANS = 384
DB = 512
CAP = 2
N_DP = 32
N_TENSOR = 8


def scaled_field(key, shape):
    key_base, key_rows, key_cols = jax.random.split(key, 3)
    row_shape = shape[:-1] + (1,)
    col_shape = (1,) * (len(shape) - 1) + (shape[-1],)
    rows_scale = jnp.exp(jax.random.uniform(key_rows, row_shape, jnp.float32, math.log(0.3), math.log(3.0)))
    cols_scale = jnp.exp(jax.random.uniform(key_cols, col_shape, jnp.float32, math.log(0.3), math.log(3.0)))
    base = jnp.clip(jax.random.normal(key_base, shape, jnp.float32), -4.0, 4.0)
    return base * rows_scale * cols_scale


def draw_hidden_states(key, part):
    return scaled_field(key, (TOKENS, D)).astype(jnp.bfloat16)


def draw_database(key, part):
    return scaled_field(key, (DB, NTOK, E)).astype(jnp.bfloat16)


def draw_neighbour_ids(key, part):
    key_hot, key_blocks, key_local = jax.random.split(jax.random.fold_in(key, 7), 3)
    request_count = CH * KN
    favourite = jax.random.randint(key_hot, (), 0, N_DP)

    def one_block(block_key):
        key_order, key_rest, key_mix = jax.random.split(block_key, 3)
        order = jax.random.permutation(key_order, N_DP)
        order = order[jnp.argsort((order != favourite).astype(jnp.int32), stable=True)]
        owner_pool = jnp.repeat(order, CAP)
        remainder = jax.random.permutation(key_rest, owner_pool[CAP:])
        chosen = jnp.concatenate([owner_pool[:CAP], remainder])[:request_count]
        return jax.random.permutation(key_mix, chosen)
    owners = jax.vmap(one_block)(jax.random.split(key_blocks, N_DP))
    local_rows = jax.random.randint(key_local, (N_DP, request_count), 0, DB_DEV)
    return (owners * DB_DEV + local_rows).reshape(SPANS, KN).astype(jnp.int32)


def block_levels(rng, dims, pieces, smallest, largest):
    gain = 1.0
    for dim, blocks in pieces:
        draws = jax.random.uniform(jax.random.fold_in(jax.random.fold_in(rng, 6), dim), (blocks,), jnp.float32, smallest / len(pieces), largest / len(pieces))
        gain = gain * jnp.repeat(jnp.exp(draws), dims[dim] // blocks).reshape((-1,) + (1,) * (len(dims) - 1 - dim))
    return gain


def centred(own_key, shape, spread, limit, cuts=(), held_as=jnp.bfloat16):
    loudness = block_levels(own_key, shape, cuts, -0.22, 0.18) if cuts else 1.0
    values = jax.random.normal(own_key, shape, jnp.float32) * spread * loudness
    return jnp.minimum(jnp.maximum(values, -limit), limit).astype(held_as)


def setup_inputs(seed: int = 0) -> dict:
    arg_keys = jax.random.split(jax.random.key(seed), 9)
    hidden_states = draw_hidden_states(jax.random.fold_in(arg_keys[8], 71), 0)
    neighbour_ids = draw_neighbour_ids(jax.random.fold_in(arg_keys[8], 71), 0)
    database = draw_database(jax.random.fold_in(arg_keys[8], 71), 0)
    w_up = centred(arg_keys[3], (E, FF), E ** -0.5, 0.1875, ((1, 8),))
    w_down = centred(arg_keys[4], (FF, E), FF ** -0.5, 0.09375, ((0, 8),))
    w_query = centred(arg_keys[5], (D, D), D ** -0.5, 0.09375, ((1, 8),))
    w_key = centred(arg_keys[6], (E, D), E ** -0.5, 0.1875, ((1, 8),))
    w_value = centred(arg_keys[7], (E, D), E ** -0.5, 0.1875, ((1, 8),))
    return dict(hidden_states=hidden_states, neighbour_ids=neighbour_ids, database=database, w_up=w_up, w_down=w_down, w_query=w_query, w_key=w_key, w_value=w_value)


EPSILON = 1e-06
LOGIT_SCALE = 3.0

def head_norm(projected):
    shaped = projected.reshape(projected.shape[0], -1, HD)
    scaled = shaped * lax.rsqrt(lax.optimization_barrier(jnp.mean(shaped * shaped, axis=-1, keepdims=True)) + EPSILON)
    return scaled.astype(jnp.bfloat16)

def attend(queries, keys, values):
    seq_rows = queries.shape[0]
    heads_here = queries.shape[1]
    span_count = seq_rows // SPAN
    shifted = jnp.concatenate([queries[SPAN - 1:], jnp.zeros((SPAN - 1, heads_here, HD), jnp.bfloat16)], axis=0)
    windows = shifted.reshape(span_count, SPAN, heads_here, HD)
    key_blocks = keys.reshape(span_count, KN * NTOK, heads_here, HD)
    value_blocks = values.reshape(span_count, KN * NTOK, heads_here, HD)
    scores = jnp.einsum('cqhd,ckhd->chqk', windows.astype(jnp.float32), key_blocks.astype(jnp.float32))
    scores = scores * (LOGIT_SCALE / math.sqrt(HD))
    expo = jnp.exp(scores)
    weights = (expo / lax.optimization_barrier(jnp.sum(expo, axis=-1, keepdims=True))).astype(jnp.bfloat16)
    mixed = jnp.einsum('chqk,ckhd->cqhd', weights.astype(jnp.float32), value_blocks.astype(jnp.float32))
    mixed = mixed.astype(jnp.bfloat16).reshape(seq_rows, heads_here * HD)
    leading = jnp.zeros((SPAN - 1, heads_here * HD), jnp.bfloat16)
    return jnp.concatenate([leading, mixed[:seq_rows - SPAN + 1]], axis=0)

def reference(hidden_states, neighbour_ids, database, w_up, w_down, w_query, w_key, w_value):

    def one_sequence(operands):
        states, chosen = operands
        blocks = database[chosen.reshape(-1)]
        raw_float = blocks.astype(jnp.float32)
        normed = (raw_float * lax.rsqrt(lax.optimization_barrier(jnp.mean(raw_float * raw_float, axis=-1, keepdims=True)) + EPSILON)).astype(jnp.bfloat16)
        inner = jnp.einsum('bte,ef->btf', normed.astype(jnp.float32), w_up.astype(jnp.float32))
        active = jax.nn.gelu(inner).astype(jnp.bfloat16)
        grouped = active.reshape(active.shape[0], NTOK, N_TENSOR, FF // N_TENSOR)
        down_grouped = w_down.reshape(N_TENSOR, FF // N_TENSOR, E)
        partials = jnp.einsum('btgf,gfe->gbte', grouped.astype(jnp.float32), down_grouped.astype(jnp.float32))
        partials = lax.optimization_barrier(partials.astype(jnp.bfloat16)).astype(jnp.float32)
        encoded = (raw_float + lax.optimization_barrier(jnp.sum(partials, axis=0))).astype(jnp.bfloat16)
        flat_encoded = encoded.reshape(-1, E)
        keys = head_norm(jnp.dot(flat_encoded, w_key, preferred_element_type=jnp.float32))
        values = jnp.dot(flat_encoded, w_value, preferred_element_type=jnp.float32).astype(jnp.bfloat16)
        values = values.reshape(flat_encoded.shape[0], HEADS, HD)
        queries = head_norm(jnp.dot(states, w_query, preferred_element_type=jnp.float32))
        return attend(queries, keys, values)
    states_all = hidden_states.reshape(N_DP, SEQ, D)
    chosen_all = neighbour_ids.reshape(N_DP, CH, KN)
    result = lax.map(one_sequence, (states_all, chosen_all))
    return result.reshape(TOKENS, D)
```

```python
import math

import jax
import jax.numpy as jnp
from jax import lax
from jax.sharding import PartitionSpec as P

HD = 128
SPAN = 64
KN = 2
NTOK = 128


EPSILON = 1e-06
LOGIT_SCALE = 3.0


def head_norm(projected):
    shaped = projected.reshape(projected.shape[0], -1, HD)
    scaled = shaped * lax.rsqrt(jnp.mean(shaped * shaped, axis=-1, keepdims=True) + EPSILON)
    return scaled.astype(jnp.bfloat16)


def attend(queries, keys, values):
    seq_rows = queries.shape[0]
    heads_here = queries.shape[1]
    span_count = seq_rows // SPAN
    shifted = jnp.concatenate(
        [queries[SPAN - 1 :], jnp.zeros((SPAN - 1, heads_here, HD), jnp.bfloat16)], axis=0
    )
    windows = shifted.reshape(span_count, SPAN, heads_here, HD)
    key_blocks = keys.reshape(span_count, KN * NTOK, heads_here, HD)
    value_blocks = values.reshape(span_count, KN * NTOK, heads_here, HD)
    scores = jnp.einsum("cqhd,ckhd->chqk", windows, key_blocks, preferred_element_type=jnp.float32)
    scores = scores * (LOGIT_SCALE / math.sqrt(HD))
    expo = jnp.exp(scores)
    weights = (expo / jnp.sum(expo, axis=-1, keepdims=True)).astype(jnp.bfloat16)
    mixed = jnp.einsum("chqk,ckhd->cqhd", weights, value_blocks, preferred_element_type=jnp.float32)
    mixed = mixed.astype(jnp.bfloat16).reshape(seq_rows, heads_here * HD)
    leading = jnp.zeros((SPAN - 1, heads_here * HD), jnp.bfloat16)
    return jnp.concatenate([leading, mixed[: seq_rows - SPAN + 1]], axis=0)


def shards(hidden_states, neighbour_ids, database, w_up, w_down, w_query, w_key, w_value):
    dp_count = lax.axis_size("dp")
    tensor_count = lax.axis_size("tensor")
    shard_blocks = database.shape[0]
    block_tokens = database.shape[1]
    enc_width = database.shape[2]
    flat_ids = neighbour_ids.reshape(-1)
    request_count = flat_ids.shape[0]
    capacity = max(2, (request_count + dp_count - 1) // dp_count + 1)
    owners = flat_ids // shard_blocks
    local_rows = flat_ids % shard_blocks
    owner_match = (owners[:, None] == jnp.arange(dp_count, dtype=jnp.int32)[None, :]).astype(
        jnp.int32
    )
    positions = jnp.arange(request_count, dtype=jnp.int32)
    earlier = (positions[:, None] > positions[None, :]).astype(jnp.int32)
    ranks = jnp.sum(jnp.dot(earlier, owner_match) * owner_match, axis=1)
    slots = owners * capacity + ranks
    slot_match = slots[None, :] == jnp.arange(dp_count * capacity, dtype=jnp.int32)[:, None]
    requests = jnp.sum(jnp.where(slot_match, local_rows[None, :], 0), axis=1)
    requests = requests.reshape(dp_count, capacity)
    raw_float = database.astype(jnp.float32)
    normed = (
        raw_float * lax.rsqrt(jnp.mean(raw_float * raw_float, axis=-1, keepdims=True) + EPSILON)
    ).astype(jnp.bfloat16)
    inner = jnp.einsum("bte,ef->btf", normed, w_up, preferred_element_type=jnp.float32)
    active = jax.nn.gelu(inner).astype(jnp.bfloat16)
    partial = jnp.einsum("btf,fe->bte", active, w_down, preferred_element_type=jnp.float32)
    rows_here = block_tokens // tensor_count
    summed = lax.psum_scatter(
        partial.astype(jnp.bfloat16), "tensor", scatter_dimension=1, tiled=True
    ).astype(jnp.float32)
    raw_own = lax.dynamic_slice_in_dim(
        raw_float, lax.axis_index("tensor") * rows_here, rows_here, 1
    )
    encoded_own = (raw_own + summed).astype(jnp.bfloat16)
    asked = lax.all_to_all(requests, "dp", split_axis=0, concat_axis=0, tiled=True)
    replies = lax.all_to_all(
        encoded_own[asked], "dp", split_axis=0, concat_axis=0, tiled=True
    )
    mine = replies.reshape(dp_count * capacity, rows_here, enc_width)[slots]
    encoded = lax.all_gather(mine, "tensor", axis=1, tiled=True)
    projected = jnp.dot(
        lax.all_gather(hidden_states, "tensor", axis=1, tiled=True),
        w_query,
        preferred_element_type=jnp.float32,
    )
    queries = head_norm(projected)
    flat_encoded = encoded.reshape(-1, enc_width)
    keys = head_norm(jnp.dot(flat_encoded, w_key, preferred_element_type=jnp.float32))
    values = jnp.dot(flat_encoded, w_value, preferred_element_type=jnp.float32).astype(jnp.bfloat16)
    values = values.reshape(flat_encoded.shape[0], -1, HD)
    return attend(queries, keys, values)


def solution(mesh):
    in_specs = (
        P("dp", "tensor"),
        P("dp", None),
        P("dp", None, None),
        P(None, "tensor"),
        P("tensor", None),
        P(None, "tensor"),
        P(None, "tensor"),
        P(None, "tensor"),
    )
    out_specs = P("dp", "tensor")
    return jax.shard_map(shards, mesh=mesh, in_specs=in_specs, out_specs=out_specs, check_vma=False)
```

```python
import math

import jax
import jax.numpy as jnp
from jax import lax
from jax.sharding import PartitionSpec as P

HD = 128
SPAN = 64
KN = 2
NTOK = 128


EPSILON = 1e-06
LOGIT_SCALE = 3.0


def head_norm(projected):
    shaped = projected.reshape(projected.shape[0], -1, HD)
    scaled = shaped * lax.rsqrt(jnp.mean(shaped * shaped, axis=-1, keepdims=True) + EPSILON)
    return scaled.astype(jnp.bfloat16)


def attend(queries, keys, values):
    seq_rows = queries.shape[0] + SPAN - 1
    heads_here = queries.shape[1]
    span_count = seq_rows // SPAN
    shifted = jnp.concatenate(
        [queries, jnp.zeros((SPAN - 1, heads_here, HD), jnp.bfloat16)], axis=0
    )
    windows = shifted.reshape(span_count, SPAN, heads_here, HD)
    key_blocks = keys.reshape(span_count, KN * NTOK, heads_here, HD)
    value_blocks = values.reshape(span_count, KN * NTOK, heads_here, HD)
    scores = jnp.einsum("cqhd,ckhd->chqk", windows, key_blocks, preferred_element_type=jnp.float32)
    scores = scores * (LOGIT_SCALE / math.sqrt(HD))
    expo = jnp.exp(scores)
    weights = (expo / jnp.sum(expo, axis=-1, keepdims=True)).astype(jnp.bfloat16)
    mixed = jnp.einsum("chqk,ckhd->cqhd", weights, value_blocks, preferred_element_type=jnp.float32)
    mixed = mixed.astype(jnp.bfloat16).reshape(seq_rows, heads_here * HD)
    leading = jnp.zeros((SPAN - 1, heads_here * HD), jnp.bfloat16)
    return jnp.concatenate([leading, mixed[: seq_rows - SPAN + 1]], axis=0)


def ring_hops(states, n):
    to_right = [(i, (i + 1) % n) for i in range(n)]
    to_left = [(i, (i - 1) % n) for i in range(n)]
    going_right = states
    going_left = states
    right_hops = n // 2
    left_hops = n - 1 - right_hops
    steps = []
    for hop in range(1, right_hops + 1):
        step = {}
        going_right = lax.ppermute(going_right, "tensor", to_right)
        step[(n - hop) % n] = going_right
        if hop <= left_hops:
            going_left = lax.ppermute(going_left, "tensor", to_left)
            step[hop] = going_left
        steps.append(step)
    return steps


def ring_query(got, w_query, n):
    width = got[0].shape[1]
    me = lax.axis_index("tensor")
    total = None
    for offset in range(n):
        rows = lax.dynamic_slice_in_dim(w_query, ((me + offset) % n) * width, width, 0)
        term = jnp.dot(got[offset], rows, preferred_element_type=jnp.float32)
        total = term if total is None else total + term
    return total


def shards(hidden_states, neighbour_ids, database, w_up, w_down, w_query, w_key, w_value):
    dp_count = lax.axis_size("dp")
    tensor_count = lax.axis_size("tensor")
    shard_blocks = database.shape[0]
    block_tokens = database.shape[1]
    enc_width = database.shape[2]
    flat_ids = neighbour_ids.reshape(-1)
    request_count = flat_ids.shape[0]
    capacity = max(2, (request_count + dp_count - 1) // dp_count + 1)
    owners = flat_ids // shard_blocks
    local_rows = flat_ids % shard_blocks
    owner_match = (owners[:, None] == jnp.arange(dp_count, dtype=jnp.int32)[None, :]).astype(
        jnp.int32
    )
    positions = jnp.arange(request_count, dtype=jnp.int32)
    earlier = (positions[:, None] > positions[None, :]).astype(jnp.int32)
    ranks = jnp.sum(jnp.dot(earlier, owner_match) * owner_match, axis=1)
    slots = owners * capacity + ranks
    slot_match = slots[None, :] == jnp.arange(dp_count * capacity, dtype=jnp.int32)[:, None]
    requests = jnp.sum(jnp.where(slot_match, local_rows[None, :], 0), axis=1)
    requests = requests.reshape(dp_count, capacity)
    raw_float = database.astype(jnp.float32)
    normed = (
        raw_float * lax.rsqrt(jnp.mean(raw_float * raw_float, axis=-1, keepdims=True) + EPSILON)
    ).astype(jnp.bfloat16)
    inner = jnp.einsum("bte,ef->btf", normed, w_up, preferred_element_type=jnp.float32)
    active = jax.nn.gelu(inner).astype(jnp.bfloat16)
    partial = jnp.einsum("btf,fe->bte", active, w_down, preferred_element_type=jnp.float32)
    rows_here = block_tokens // tensor_count
    summed = lax.psum_scatter(
        partial.astype(jnp.bfloat16), "tensor", scatter_dimension=1, tiled=True
    ).astype(jnp.float32)
    raw_own = lax.dynamic_slice_in_dim(
        raw_float, lax.axis_index("tensor") * rows_here, rows_here, 1
    )
    encoded_own = (raw_own + summed).astype(jnp.bfloat16)
    states = hidden_states[SPAN - 1 :]
    steps = ring_hops(states, tensor_count)
    got = {0: states}
    for step in steps:
        got.update(step)
    early = [v for step in steps[: len(steps) // 2] for v in step.values()]
    late = [v for step in steps[len(steps) // 2 :] for v in step.values()]
    asked = lax.all_to_all(requests, "dp", split_axis=0, concat_axis=0, tiled=True)
    served, _ = lax.optimization_barrier((encoded_own[asked], early))
    replies = lax.all_to_all(served, "dp", split_axis=0, concat_axis=0, tiled=True)
    mine = replies.reshape(dp_count * capacity, rows_here, enc_width)[slots]
    mine, _ = lax.optimization_barrier((mine, late))
    encoded = lax.all_gather(mine, "tensor", axis=1, tiled=True)
    queries = head_norm(ring_query(got, w_query, tensor_count))
    flat_encoded = encoded.reshape(-1, enc_width)
    keys = head_norm(jnp.dot(flat_encoded, w_key, preferred_element_type=jnp.float32))
    values = jnp.dot(flat_encoded, w_value, preferred_element_type=jnp.float32).astype(jnp.bfloat16)
    values = values.reshape(flat_encoded.shape[0], -1, HD)
    return attend(queries, keys, values)


def solution(mesh):
    in_specs = (
        P("dp", "tensor"),
        P("dp", None),
        P("dp", None, None),
        P(None, "tensor"),
        P("tensor", None),
        P(None, "tensor"),
        P(None, "tensor"),
        P(None, "tensor"),
    )
    out_specs = P("dp", "tensor")
    return jax.shard_map(shards, mesh=mesh, in_specs=in_specs, out_specs=out_specs, check_vma=False)
```

```python
import math

import jax
import jax.numpy as jnp
from jax import lax
from jax.sharding import PartitionSpec as P

HD = 128
SPAN = 64
KN = 2
NTOK = 128


EPSILON = 1e-06
LOGIT_SCALE = 3.0


def head_norm(projected):
    shaped = projected.reshape(projected.shape[0], -1, HD)
    scaled = shaped * lax.rsqrt(jnp.mean(shaped * shaped, axis=-1, keepdims=True) + EPSILON)
    return scaled.astype(jnp.bfloat16)


def attend(windows_flat, keys, values):
    heads_here = windows_flat.shape[1]
    span_count = windows_flat.shape[0] // SPAN
    windows = windows_flat.reshape(span_count, SPAN, heads_here, HD)
    key_blocks = keys.reshape(span_count, KN * NTOK, heads_here, HD)
    value_blocks = values.reshape(span_count, KN * NTOK, heads_here, HD)
    scores = jnp.einsum("cqhd,ckhd->chqk", windows, key_blocks, preferred_element_type=jnp.float32)
    scores = scores * (LOGIT_SCALE / math.sqrt(HD))
    expo = jnp.exp(scores)
    weights = (expo / jnp.sum(expo, axis=-1, keepdims=True)).astype(jnp.bfloat16)
    mixed = jnp.einsum("chqk,ckhd->cqhd", weights, value_blocks, preferred_element_type=jnp.float32)
    return mixed.astype(jnp.bfloat16).reshape(span_count * SPAN, heads_here * HD)

def ring_hops(states, n):
    to_right = [(i, (i + 1) % n) for i in range(n)]
    to_left = [(i, (i - 1) % n) for i in range(n)]
    going_right = states
    going_left = states
    right_hops = n // 2
    left_hops = n - 1 - right_hops
    steps = []
    for hop in range(1, right_hops + 1):
        step = {}
        going_right = lax.ppermute(going_right, "tensor", to_right)
        step[(n - hop) % n] = going_right
        if hop <= left_hops:
            going_left = lax.ppermute(going_left, "tensor", to_left)
            step[hop] = going_left
        steps.append(step)
    return steps


def ring_query(got, w_query, n):
    width = got[0].shape[1]
    me = lax.axis_index("tensor")
    total = None
    for offset in range(n):
        rows = lax.dynamic_slice_in_dim(w_query, ((me + offset) % n) * width, width, 0)
        term = jnp.dot(got[offset], rows, preferred_element_type=jnp.float32)
        total = term if total is None else total + term
    return total


def shards(hidden_states, neighbour_ids, database, w_up, w_down, w_query, w_key, w_value):
    dp_count = lax.axis_size("dp")
    tensor_count = lax.axis_size("tensor")
    shard_blocks = database.shape[0]
    block_tokens = database.shape[1]
    enc_width = database.shape[2]
    flat_ids = neighbour_ids.reshape(-1)
    request_count = flat_ids.shape[0]
    capacity = max(2, (request_count + dp_count - 1) // dp_count + 1)
    owners = flat_ids // shard_blocks
    local_rows = flat_ids % shard_blocks
    owner_match = (owners[:, None] == jnp.arange(dp_count, dtype=jnp.int32)[None, :]).astype(
        jnp.int32
    )
    positions = jnp.arange(request_count, dtype=jnp.int32)
    earlier = (positions[:, None] > positions[None, :]).astype(jnp.int32)
    ranks = jnp.sum(jnp.dot(earlier, owner_match) * owner_match, axis=1)
    slots = owners * capacity + ranks
    slot_match = slots[None, :] == jnp.arange(dp_count * capacity, dtype=jnp.int32)[:, None]
    requests = jnp.sum(jnp.where(slot_match, local_rows[None, :], 0), axis=1)
    requests = requests.reshape(dp_count, capacity)
    raw_float = database.astype(jnp.float32)
    normed = (
        raw_float * lax.rsqrt(jnp.mean(raw_float * raw_float, axis=-1, keepdims=True) + EPSILON)
    ).astype(jnp.bfloat16)
    inner = jnp.einsum("bte,ef->btf", normed, w_up, preferred_element_type=jnp.float32)
    active = jax.nn.gelu(inner).astype(jnp.bfloat16)
    partial = jnp.einsum("btf,fe->bte", active, w_down, preferred_element_type=jnp.float32)
    rows_here = block_tokens // tensor_count
    states = hidden_states[SPAN - 1 :]
    steps = ring_hops(states, tensor_count)
    got = {0: states}
    for step in steps:
        got.update(step)
    first = list(steps[0].values())
    middle = [v for step in steps[1 : len(steps) // 2] for v in step.values()]
    late = [v for step in steps[len(steps) // 2 :] for v in step.values()]
    partial, _ = lax.optimization_barrier((partial.astype(jnp.bfloat16), first))
    summed = lax.psum_scatter(partial, "tensor", scatter_dimension=1, tiled=True).astype(
        jnp.float32
    )
    raw_own = lax.dynamic_slice_in_dim(
        raw_float, lax.axis_index("tensor") * rows_here, rows_here, 1
    )
    encoded_own = (raw_own + summed).astype(jnp.bfloat16)
    asked = lax.all_to_all(requests, "dp", split_axis=0, concat_axis=0, tiled=True)
    served, _ = lax.optimization_barrier((encoded_own[asked], middle))
    replies = lax.all_to_all(served, "dp", split_axis=0, concat_axis=0, tiled=True)
    mine = replies.reshape(dp_count * capacity, rows_here, enc_width)[slots]
    mine, _ = lax.optimization_barrier((mine, late))
    queries = head_norm(ring_query(got, w_query, tensor_count))
    halves = 2
    block_share = request_count // halves
    query_share = queries.shape[0] + SPAN - 1
    query_share = query_share // halves
    padded = jnp.concatenate(
        [queries, jnp.zeros((SPAN - 1,) + queries.shape[1:], queries.dtype)], axis=0
    )
    mixed = []
    for half in range(halves):
        part = lax.all_gather(
            mine[half * block_share : (half + 1) * block_share], "tensor", axis=1, tiled=True
        )
        flat_encoded = part.reshape(-1, enc_width)
        keys = head_norm(jnp.dot(flat_encoded, w_key, preferred_element_type=jnp.float32))
        values = jnp.dot(flat_encoded, w_value, preferred_element_type=jnp.float32).astype(
            jnp.bfloat16
        )
        values = values.reshape(flat_encoded.shape[0], -1, HD)
        mixed.append(attend(padded[half * query_share : (half + 1) * query_share], keys, values))
    mixed = jnp.concatenate(mixed, axis=0)
    heads_width = mixed.shape[1]
    leading = jnp.zeros((SPAN - 1, heads_width), jnp.bfloat16)
    return jnp.concatenate([leading, mixed[: mixed.shape[0] - SPAN + 1]], axis=0)


def solution(mesh):
    in_specs = (
        P("dp", "tensor"),
        P("dp", None),
        P("dp", None, None),
        P(None, "tensor"),
        P("tensor", None),
        P(None, "tensor"),
        P(None, "tensor"),
        P(None, "tensor"),
    )
    out_specs = P("dp", "tensor")
    return jax.shard_map(shards, mesh=mesh, in_specs=in_specs, out_specs=out_specs, check_vma=False)
```

```python
import math

import jax
import jax.numpy as jnp
from jax import lax
from jax.sharding import PartitionSpec as P

HD = 128
SPAN = 64
KN = 2
NTOK = 128


EPSILON = 1e-06
LOGIT_SCALE = 3.0


def head_norm(projected):
    shaped = projected.reshape(projected.shape[0], -1, HD)
    scaled = shaped * lax.rsqrt(jnp.mean(shaped * shaped, axis=-1, keepdims=True) + EPSILON)
    return scaled.astype(jnp.bfloat16)


def attend(windows_flat, keys, values):
    heads_here = windows_flat.shape[1]
    span_count = windows_flat.shape[0] // SPAN
    windows = windows_flat.reshape(span_count, SPAN, heads_here, HD)
    key_blocks = keys.reshape(span_count, KN * NTOK, heads_here, HD)
    value_blocks = values.reshape(span_count, KN * NTOK, heads_here, HD)
    scores = jnp.einsum("cqhd,ckhd->chqk", windows, key_blocks, preferred_element_type=jnp.float32)
    scores = scores * (LOGIT_SCALE / math.sqrt(HD))
    expo = jnp.exp(scores)
    weights = (expo / jnp.sum(expo, axis=-1, keepdims=True)).astype(jnp.bfloat16)
    mixed = jnp.einsum("chqk,ckhd->cqhd", weights, value_blocks, preferred_element_type=jnp.float32)
    return mixed.astype(jnp.bfloat16).reshape(span_count * SPAN, heads_here * HD)

def ring_hops(states, n):
    to_right = [(i, (i + 1) % n) for i in range(n)]
    to_left = [(i, (i - 1) % n) for i in range(n)]
    going_right = states
    going_left = states
    right_hops = n // 2
    left_hops = n - 1 - right_hops
    steps = []
    for hop in range(1, right_hops + 1):
        step = {}
        going_right = lax.ppermute(going_right, "tensor", to_right)
        step[(n - hop) % n] = going_right
        if hop <= left_hops:
            going_left = lax.ppermute(going_left, "tensor", to_left)
            step[hop] = going_left
        steps.append(step)
    return steps


def ring_query(got, w_query, n):
    width = got[0].shape[1]
    me = lax.axis_index("tensor")
    total = None
    for offset in range(n):
        rows = lax.dynamic_slice_in_dim(w_query, ((me + offset) % n) * width, width, 0)
        term = jnp.dot(got[offset], rows, preferred_element_type=jnp.float32)
        total = term if total is None else total + term
    return total


def shards(hidden_states, neighbour_ids, database, w_up, w_down, w_query, w_key, w_value):
    dp_count = lax.axis_size("dp")
    tensor_count = lax.axis_size("tensor")
    shard_blocks = database.shape[0]
    block_tokens = database.shape[1]
    enc_width = database.shape[2]
    flat_ids = neighbour_ids.reshape(-1)
    request_count = flat_ids.shape[0]
    capacity = max(2, (request_count + dp_count - 1) // dp_count + 1)
    owners = flat_ids // shard_blocks
    local_rows = flat_ids % shard_blocks
    owner_match = (owners[:, None] == jnp.arange(dp_count, dtype=jnp.int32)[None, :]).astype(
        jnp.int32
    )
    positions = jnp.arange(request_count, dtype=jnp.int32)
    earlier = (positions[:, None] > positions[None, :]).astype(jnp.int32)
    ranks = jnp.sum(jnp.dot(earlier, owner_match) * owner_match, axis=1)
    slots = owners * capacity + ranks
    slot_match = slots[None, :] == jnp.arange(dp_count * capacity, dtype=jnp.int32)[:, None]
    requests = jnp.sum(jnp.where(slot_match, local_rows[None, :], 0), axis=1)
    requests = requests.reshape(dp_count, capacity)
    pieces = dp_count
    me_dp = lax.axis_index("dp")
    up_piece = lax.dynamic_slice_in_dim(w_up, me_dp * (w_up.shape[0] // pieces), w_up.shape[0] // pieces, 0)
    down_piece = lax.dynamic_slice_in_dim(
        w_down, me_dp * (w_down.shape[0] // pieces), w_down.shape[0] // pieces, 0
    )
    up_all = lax.all_gather(lax.all_gather(up_piece, "tensor"), "dp")
    down_all = lax.all_gather(lax.all_gather(down_piece, "tensor"), "dp")
    rows_here = block_tokens // tensor_count
    raw_float = database.astype(jnp.float32)
    raw_own = lax.dynamic_slice_in_dim(
        raw_float, lax.axis_index("tensor") * rows_here, rows_here, 1
    )
    normed = (
        raw_own * lax.rsqrt(jnp.mean(raw_own * raw_own, axis=-1, keepdims=True) + EPSILON)
    ).astype(jnp.bfloat16)
    states = hidden_states[SPAN - 1 :]
    steps = ring_hops(states, tensor_count)
    got = {0: states}
    for step in steps:
        got.update(step)
    early = [v for step in steps[: len(steps) // 2] for v in step.values()]
    late = [v for step in steps[len(steps) // 2 :] for v in step.values()]
    normed, _ = lax.optimization_barrier((normed, early))
    flat_normed = normed.reshape(shard_blocks * rows_here, pieces, enc_width // pieces)
    inner = jnp.einsum("ncr,cgrh->ngh", flat_normed, up_all, preferred_element_type=jnp.float32)
    active = jax.nn.gelu(inner).astype(jnp.bfloat16)
    active = active.reshape(active.shape[0], tensor_count, pieces, -1)
    partials = jnp.einsum("ngcr,cgre->gne", active, down_all, preferred_element_type=jnp.float32)
    summed = jnp.sum(partials.astype(jnp.bfloat16).astype(jnp.float32), axis=0)
    summed = summed.reshape(shard_blocks, rows_here, enc_width)
    encoded_own = (raw_own + summed).astype(jnp.bfloat16)
    asked = lax.all_to_all(requests, "dp", split_axis=0, concat_axis=0, tiled=True)
    served, _ = lax.optimization_barrier((encoded_own[asked], late))
    replies = lax.all_to_all(served, "dp", split_axis=0, concat_axis=0, tiled=True)
    mine = replies.reshape(dp_count * capacity, rows_here, enc_width)[slots]
    queries = head_norm(ring_query(got, w_query, tensor_count))
    padded = jnp.concatenate(
        [queries, jnp.zeros((SPAN - 1,) + queries.shape[1:], queries.dtype)], axis=0
    )
    encoded = lax.all_gather(mine, "tensor", axis=1, tiled=True)
    flat_encoded = encoded.reshape(-1, enc_width)
    keys = head_norm(jnp.dot(flat_encoded, w_key, preferred_element_type=jnp.float32))
    values = jnp.dot(flat_encoded, w_value, preferred_element_type=jnp.float32).astype(
        jnp.bfloat16
    )
    values = values.reshape(flat_encoded.shape[0], -1, HD)
    mixed = [attend(padded, keys, values)]
    mixed = jnp.concatenate(mixed, axis=0)
    heads_width = mixed.shape[1]
    leading = jnp.zeros((SPAN - 1, heads_width), jnp.bfloat16)
    return jnp.concatenate([leading, mixed[: mixed.shape[0] - SPAN + 1]], axis=0)


def solution(mesh):
    in_specs = (
        P("dp", "tensor"),
        P("dp", None),
        P("dp", None, None),
        P(None, "tensor"),
        P("tensor", None),
        P(None, "tensor"),
        P(None, "tensor"),
        P(None, "tensor"),
    )
    out_specs = P("dp", "tensor")
    return jax.shard_map(shards, mesh=mesh, in_specs=in_specs, out_specs=out_specs, check_vma=False)
```

```python
import math

import jax
import jax.numpy as jnp
from jax import lax
from jax.sharding import PartitionSpec as P

HD = 128
SPAN = 64
KN = 2
NTOK = 128


EPSILON = 1e-06
LOGIT_SCALE = 3.0


def head_norm(projected):
    shaped = projected.reshape(projected.shape[0], -1, HD)
    scaled = shaped * lax.rsqrt(jnp.mean(shaped * shaped, axis=-1, keepdims=True) + EPSILON)
    return scaled.astype(jnp.bfloat16)


def attend(queries, keys, values):
    heads_here = queries.shape[0]
    seq_rows = queries.shape[1] + SPAN - 1
    span_count = seq_rows // SPAN
    shifted = jnp.concatenate(
        [queries, jnp.zeros((heads_here, SPAN - 1, HD), jnp.bfloat16)], axis=1
    )
    windows = shifted.reshape(heads_here, span_count, SPAN, HD)
    key_blocks = keys.reshape(heads_here, span_count, KN * NTOK, HD)
    value_blocks = values.reshape(heads_here, span_count, KN * NTOK, HD)
    scores = jnp.einsum("hcqd,hckd->hcqk", windows, key_blocks, preferred_element_type=jnp.float32)
    scores = scores * (LOGIT_SCALE / math.sqrt(HD))
    expo = jnp.exp(scores)
    weights = (expo / jnp.sum(expo, axis=-1, keepdims=True)).astype(jnp.bfloat16)
    mixed = jnp.einsum("hcqk,hckd->cqhd", weights, value_blocks, preferred_element_type=jnp.float32)
    mixed = mixed.astype(jnp.bfloat16).reshape(seq_rows, heads_here * HD)
    leading = jnp.zeros((SPAN - 1, heads_here * HD), jnp.bfloat16)
    return jnp.concatenate([leading, mixed[: seq_rows - SPAN + 1]], axis=0)


def head_norm_major(projected):
    scaled = projected * lax.rsqrt(jnp.mean(projected * projected, axis=-1, keepdims=True) + EPSILON)
    return scaled.astype(jnp.bfloat16)

def shards(hidden_states, neighbour_ids, database, w_up, w_down, w_query, w_key, w_value):
    dp_count = lax.axis_size("dp")
    tensor_count = lax.axis_size("tensor")
    shard_blocks = database.shape[0]
    block_tokens = database.shape[1]
    enc_width = database.shape[2]
    flat_ids = neighbour_ids.reshape(-1)
    request_count = flat_ids.shape[0]
    capacity = max(2, (request_count + dp_count - 1) // dp_count + 1)
    owners = flat_ids // shard_blocks
    local_rows = flat_ids % shard_blocks
    owner_match = (owners[:, None] == jnp.arange(dp_count, dtype=jnp.int32)[None, :]).astype(
        jnp.int32
    )
    positions = jnp.arange(request_count, dtype=jnp.int32)
    earlier = (positions[:, None] > positions[None, :]).astype(jnp.int32)
    ranks = jnp.sum(jnp.dot(earlier, owner_match) * owner_match, axis=1)
    slots = owners * capacity + ranks
    slot_match = slots[None, :] == jnp.arange(dp_count * capacity, dtype=jnp.int32)[:, None]
    requests = jnp.sum(jnp.where(slot_match, local_rows[None, :], 0), axis=1)
    requests = requests.reshape(dp_count, capacity)
    raw_float = database.astype(jnp.float32)
    normed = (
        raw_float * lax.rsqrt(jnp.mean(raw_float * raw_float, axis=-1, keepdims=True) + EPSILON)
    ).astype(jnp.bfloat16)
    inner = jnp.einsum("bte,ef->btf", normed, w_up, preferred_element_type=jnp.float32)
    active = jax.nn.gelu(inner).astype(jnp.bfloat16)
    partial = jnp.einsum("btf,fe->bte", active, w_down, preferred_element_type=jnp.float32)
    rows_here = block_tokens // tensor_count
    summed = lax.psum_scatter(
        partial.astype(jnp.bfloat16), "tensor", scatter_dimension=1, tiled=True
    ).astype(jnp.float32)
    raw_own = lax.dynamic_slice_in_dim(
        raw_float, lax.axis_index("tensor") * rows_here, rows_here, 1
    )
    encoded_own = (raw_own + summed).astype(jnp.bfloat16)
    asked = lax.all_to_all(requests, "dp", split_axis=0, concat_axis=0, tiled=True)
    replies = lax.all_to_all(
        encoded_own[asked], "dp", split_axis=0, concat_axis=0, tiled=True
    )
    mine = replies.reshape(dp_count * capacity, rows_here, enc_width)[slots]
    encoded = lax.all_gather(mine, "tensor", axis=1, tiled=True)
    heads_here = w_query.shape[1] // HD
    projected = jnp.dot(
        lax.all_gather(hidden_states[SPAN - 1 :], "tensor", axis=1, tiled=True),
        w_query,
        preferred_element_type=jnp.float32,
    )
    queries = head_norm_major(projected.reshape(projected.shape[0], heads_here, HD))
    queries = jnp.transpose(queries, (1, 0, 2))
    flat_encoded = encoded.reshape(-1, enc_width)
    keys = head_norm_major(
        jnp.einsum(
            "ke,ehd->hkd",
            flat_encoded,
            w_key.reshape(enc_width, heads_here, HD),
            preferred_element_type=jnp.float32,
        )
    )
    values = jnp.einsum(
        "ke,ehd->hkd",
        flat_encoded,
        w_value.reshape(enc_width, heads_here, HD),
        preferred_element_type=jnp.float32,
    ).astype(jnp.bfloat16)
    return attend(queries, keys, values)

def solution(mesh):
    in_specs = (
        P("dp", "tensor"),
        P("dp", None),
        P("dp", None, None),
        P(None, "tensor"),
        P("tensor", None),
        P(None, "tensor"),
        P(None, "tensor"),
        P(None, "tensor"),
    )
    out_specs = P("dp", "tensor")
    return jax.shard_map(shards, mesh=mesh, in_specs=in_specs, out_specs=out_specs, check_vma=False)
```

```python
import math

import jax
import jax.numpy as jnp
from jax import lax
from jax.sharding import PartitionSpec as P

HD = 128
SPAN = 64
KN = 2
NTOK = 128


EPSILON = 1e-06
LOGIT_SCALE = 3.0


def head_norm(projected):
    shaped = projected.reshape(projected.shape[0], -1, HD)
    scaled = shaped * lax.rsqrt(jnp.mean(shaped * shaped, axis=-1, keepdims=True) + EPSILON)
    return scaled.astype(jnp.bfloat16)


def attend(queries, keys, values):
    heads_here = queries.shape[0]
    seq_rows = queries.shape[1] + SPAN - 1
    span_count = seq_rows // SPAN
    shifted = jnp.concatenate(
        [queries, jnp.zeros((heads_here, SPAN - 1, HD), jnp.bfloat16)], axis=1
    )
    windows = shifted.reshape(heads_here, span_count, SPAN, HD)
    key_blocks = keys.reshape(heads_here, span_count, KN * NTOK, HD)
    value_blocks = values.reshape(heads_here, span_count, KN * NTOK, HD)
    scores = jnp.einsum("hcqd,hckd->hcqk", windows, key_blocks, preferred_element_type=jnp.float32)
    scores = scores * (LOGIT_SCALE / math.sqrt(HD))
    expo = jnp.exp(scores)
    weights = (expo / jnp.sum(expo, axis=-1, keepdims=True)).astype(jnp.bfloat16)
    mixed = jnp.einsum("hcqk,hckd->cqhd", weights, value_blocks, preferred_element_type=jnp.float32)
    mixed = mixed.astype(jnp.bfloat16).reshape(seq_rows, heads_here * HD)
    leading = jnp.zeros((SPAN - 1, heads_here * HD), jnp.bfloat16)
    return jnp.concatenate([leading, mixed[: seq_rows - SPAN + 1]], axis=0)


def head_norm_major(projected):
    scaled = projected * lax.rsqrt(jnp.mean(projected * projected, axis=-1, keepdims=True) + EPSILON)
    return scaled.astype(jnp.bfloat16)

def ring_hops(states, n):
    to_right = [(i, (i + 1) % n) for i in range(n)]
    to_left = [(i, (i - 1) % n) for i in range(n)]
    going_right = states
    going_left = states
    right_hops = n // 2
    left_hops = n - 1 - right_hops
    steps = []
    for hop in range(1, right_hops + 1):
        step = {}
        going_right = lax.ppermute(going_right, "tensor", to_right)
        step[(n - hop) % n] = going_right
        if hop <= left_hops:
            going_left = lax.ppermute(going_left, "tensor", to_left)
            step[hop] = going_left
        steps.append(step)
    return steps


def ring_query(got, w_query, n):
    width = got[0].shape[1]
    me = lax.axis_index("tensor")
    total = None
    for offset in range(n):
        rows = lax.dynamic_slice_in_dim(w_query, ((me + offset) % n) * width, width, 0)
        term = jnp.dot(got[offset], rows, preferred_element_type=jnp.float32)
        total = term if total is None else total + term
    return total


def shards(hidden_states, neighbour_ids, database, w_up, w_down, w_query, w_key, w_value):
    dp_count = lax.axis_size("dp")
    tensor_count = lax.axis_size("tensor")
    shard_blocks = database.shape[0]
    block_tokens = database.shape[1]
    enc_width = database.shape[2]
    flat_ids = neighbour_ids.reshape(-1)
    request_count = flat_ids.shape[0]
    capacity = max(2, (request_count + dp_count - 1) // dp_count + 1)
    owners = flat_ids // shard_blocks
    local_rows = flat_ids % shard_blocks
    owner_match = (owners[:, None] == jnp.arange(dp_count, dtype=jnp.int32)[None, :]).astype(
        jnp.int32
    )
    positions = jnp.arange(request_count, dtype=jnp.int32)
    earlier = (positions[:, None] > positions[None, :]).astype(jnp.int32)
    ranks = jnp.sum(jnp.dot(earlier, owner_match) * owner_match, axis=1)
    slots = owners * capacity + ranks
    slot_match = slots[None, :] == jnp.arange(dp_count * capacity, dtype=jnp.int32)[:, None]
    requests = jnp.sum(jnp.where(slot_match, local_rows[None, :], 0), axis=1)
    requests = requests.reshape(dp_count, capacity)
    raw_float = database.astype(jnp.float32)
    normed = (
        raw_float * lax.rsqrt(jnp.mean(raw_float * raw_float, axis=-1, keepdims=True) + EPSILON)
    ).astype(jnp.bfloat16)
    inner = jnp.einsum("bte,ef->btf", normed, w_up, preferred_element_type=jnp.float32)
    active = jax.nn.gelu(inner).astype(jnp.bfloat16)
    partial = jnp.einsum("btf,fe->bte", active, w_down, preferred_element_type=jnp.float32)
    rows_here = block_tokens // tensor_count
    states = hidden_states[SPAN - 1 :]
    head_rows = SPAN
    head_got = {0: states[:head_rows]}
    for step in ring_hops(states[:head_rows], tensor_count):
        head_got.update(step)
    summed = lax.psum_scatter(
        partial.astype(jnp.bfloat16), "tensor", scatter_dimension=1, tiled=True
    )
    states_rest, summed = lax.optimization_barrier((states[head_rows:], summed))
    summed = summed.astype(jnp.float32)
    raw_own = lax.dynamic_slice_in_dim(
        raw_float, lax.axis_index("tensor") * rows_here, rows_here, 1
    )
    encoded_own = (raw_own + summed).astype(jnp.bfloat16)
    asked = lax.all_to_all(requests, "dp", split_axis=0, concat_axis=0, tiled=True)
    served, head_got = lax.optimization_barrier((encoded_own[asked], head_got))
    replies = lax.all_to_all(served, "dp", split_axis=0, concat_axis=0, tiled=True)
    mine = replies.reshape(dp_count * capacity, rows_here, enc_width)[slots]
    encoded = lax.all_gather(mine, "tensor", axis=1, tiled=True)
    heads_here = w_query.shape[1] // HD
    states_rest = lax.all_gather(states_rest, "tensor", axis=1, tiled=True)
    projected = jnp.concatenate(
        [
            ring_query(head_got, w_query, tensor_count),
            jnp.dot(states_rest, w_query, preferred_element_type=jnp.float32),
        ],
        axis=0,
    )
    queries = head_norm_major(projected.reshape(projected.shape[0], heads_here, HD))
    queries = jnp.transpose(queries, (1, 0, 2))
    flat_encoded = encoded.reshape(-1, enc_width)
    keys = head_norm_major(
        jnp.einsum(
            "ke,ehd->hkd",
            flat_encoded,
            w_key.reshape(enc_width, heads_here, HD),
            preferred_element_type=jnp.float32,
        )
    )
    values = jnp.einsum(
        "ke,ehd->hkd",
        flat_encoded,
        w_value.reshape(enc_width, heads_here, HD),
        preferred_element_type=jnp.float32,
    ).astype(jnp.bfloat16)
    return attend(queries, keys, values)

def solution(mesh):
    in_specs = (
        P("dp", "tensor"),
        P("dp", None),
        P("dp", None, None),
        P(None, "tensor"),
        P("tensor", None),
        P(None, "tensor"),
        P(None, "tensor"),
        P(None, "tensor"),
    )
    out_specs = P("dp", "tensor")
    return jax.shard_map(shards, mesh=mesh, in_specs=in_specs, out_specs=out_specs, check_vma=False)
```

```python
import math

import jax
import jax.numpy as jnp
from jax import lax
from jax.sharding import PartitionSpec as P

HD = 128
SPAN = 64
KN = 2
NTOK = 128


EPSILON = 1e-06
LOGIT_SCALE = 3.0


def head_norm(projected):
    shaped = projected.reshape(projected.shape[0], -1, HD)
    scaled = shaped * lax.rsqrt(jnp.mean(shaped * shaped, axis=-1, keepdims=True) + EPSILON)
    return scaled.astype(jnp.bfloat16)


def attend(queries, keys, values):
    heads_here = queries.shape[0]
    seq_rows = queries.shape[1] + SPAN - 1
    span_count = seq_rows // SPAN
    shifted = jnp.concatenate(
        [queries, jnp.zeros((heads_here, SPAN - 1, HD), jnp.bfloat16)], axis=1
    )
    windows = shifted.reshape(heads_here, span_count, SPAN, HD)
    key_blocks = keys.reshape(heads_here, span_count, KN * NTOK, HD)
    value_blocks = values.reshape(heads_here, span_count, KN * NTOK, HD)
    scores = jnp.einsum("hcqd,hckd->hcqk", windows, key_blocks, preferred_element_type=jnp.float32)
    scores = scores * (LOGIT_SCALE / math.sqrt(HD))
    expo = jnp.exp(scores)
    weights = (expo / jnp.sum(expo, axis=-1, keepdims=True)).astype(jnp.bfloat16)
    mixed = jnp.einsum("hcqk,hckd->cqhd", weights, value_blocks, preferred_element_type=jnp.float32)
    mixed = mixed.astype(jnp.bfloat16).reshape(seq_rows, heads_here * HD)
    leading = jnp.zeros((SPAN - 1, heads_here * HD), jnp.bfloat16)
    return jnp.concatenate([leading, mixed[: seq_rows - SPAN + 1]], axis=0)


def head_norm_major(projected):
    scaled = projected * lax.rsqrt(jnp.mean(projected * projected, axis=-1, keepdims=True) + EPSILON)
    return scaled.astype(jnp.bfloat16)

def shards(hidden_states, neighbour_ids, database, w_up, w_down, w_query, w_key, w_value):
    dp_count = lax.axis_size("dp")
    tensor_count = lax.axis_size("tensor")
    shard_blocks = database.shape[0]
    block_tokens = database.shape[1]
    enc_width = database.shape[2]
    flat_ids = neighbour_ids.reshape(-1)
    request_count = flat_ids.shape[0]
    capacity = max(2, (request_count + dp_count - 1) // dp_count + 1)
    owners = flat_ids // shard_blocks
    local_rows = flat_ids % shard_blocks
    owner_match = (owners[:, None] == jnp.arange(dp_count, dtype=jnp.int32)[None, :]).astype(
        jnp.int32
    )
    positions = jnp.arange(request_count, dtype=jnp.int32)
    earlier = (positions[:, None] > positions[None, :]).astype(jnp.int32)
    ranks = jnp.sum(jnp.dot(earlier, owner_match) * owner_match, axis=1)
    slots = owners * capacity + ranks
    slot_match = slots[None, :] == jnp.arange(dp_count * capacity, dtype=jnp.int32)[:, None]
    requests = jnp.sum(jnp.where(slot_match, local_rows[None, :], 0), axis=1)
    requests = requests.reshape(dp_count, capacity)
    raw_float = database.astype(jnp.float32)
    normed = (
        raw_float * lax.rsqrt(jnp.mean(raw_float * raw_float, axis=-1, keepdims=True) + EPSILON)
    ).astype(jnp.bfloat16)
    inner = jnp.einsum("bte,ef->btf", normed, w_up, preferred_element_type=jnp.float32)
    active = jax.nn.gelu(inner).astype(jnp.bfloat16)
    partial = jnp.einsum("btf,fe->bte", active, w_down, preferred_element_type=jnp.float32)
    rows_here = block_tokens // tensor_count
    states = hidden_states[SPAN - 1 :]
    head_rows = 2 * SPAN
    states_head = lax.all_gather(states[:head_rows], "tensor", axis=1, tiled=True)
    partial, states_head = lax.optimization_barrier((partial.astype(jnp.bfloat16), states_head))
    summed = lax.psum_scatter(partial, "tensor", scatter_dimension=1, tiled=True)
    states_rest, summed = lax.optimization_barrier((states[head_rows:], summed))
    summed = summed.astype(jnp.float32)
    raw_own = lax.dynamic_slice_in_dim(
        raw_float, lax.axis_index("tensor") * rows_here, rows_here, 1
    )
    encoded_own = (raw_own + summed).astype(jnp.bfloat16)
    asked = lax.all_to_all(requests, "dp", split_axis=0, concat_axis=0, tiled=True)
    replies = lax.all_to_all(
        encoded_own[asked], "dp", split_axis=0, concat_axis=0, tiled=True
    )
    mine = replies.reshape(dp_count * capacity, rows_here, enc_width)[slots]
    encoded = lax.all_gather(mine, "tensor", axis=1, tiled=True)
    heads_here = w_query.shape[1] // HD
    states_rest = lax.all_gather(states_rest, "tensor", axis=1, tiled=True)
    projected = jnp.concatenate(
        [
            jnp.dot(states_head, w_query, preferred_element_type=jnp.float32),
            jnp.dot(states_rest, w_query, preferred_element_type=jnp.float32),
        ],
        axis=0,
    )
    queries = head_norm_major(projected.reshape(projected.shape[0], heads_here, HD))
    queries = jnp.transpose(queries, (1, 0, 2))
    flat_encoded = encoded.reshape(-1, enc_width)
    keys = head_norm_major(
        jnp.einsum(
            "ke,ehd->hkd",
            flat_encoded,
            w_key.reshape(enc_width, heads_here, HD),
            preferred_element_type=jnp.float32,
        )
    )
    values = jnp.einsum(
        "ke,ehd->hkd",
        flat_encoded,
        w_value.reshape(enc_width, heads_here, HD),
        preferred_element_type=jnp.float32,
    ).astype(jnp.bfloat16)
    return attend(queries, keys, values)

def solution(mesh):
    in_specs = (
        P("dp", "tensor"),
        P("dp", None),
        P("dp", None, None),
        P(None, "tensor"),
        P("tensor", None),
        P(None, "tensor"),
        P(None, "tensor"),
        P(None, "tensor"),
    )
    out_specs = P("dp", "tensor")
    return jax.shard_map(shards, mesh=mesh, in_specs=in_specs, out_specs=out_specs, check_vma=False)
```

```python
import math

import jax
import jax.numpy as jnp
from jax import lax
from jax.sharding import PartitionSpec as P

HD = 128
SPAN = 64
KN = 2
NTOK = 128


EPSILON = 1e-06
LOGIT_SCALE = 3.0


def head_norm(projected):
    shaped = projected.reshape(projected.shape[0], -1, HD)
    scaled = shaped * lax.rsqrt(jnp.mean(shaped * shaped, axis=-1, keepdims=True) + EPSILON)
    return scaled.astype(jnp.bfloat16)


def attend(queries, keys, key_scale, values):
    heads_here = queries.shape[0]
    seq_rows = queries.shape[1] + SPAN - 1
    span_count = seq_rows // SPAN
    shifted = jnp.concatenate(
        [queries, jnp.zeros((heads_here, SPAN - 1, HD), jnp.bfloat16)], axis=1
    )
    windows = shifted.reshape(heads_here, span_count, SPAN, HD)
    key_blocks = keys.reshape(heads_here, span_count, KN * NTOK, HD)
    key_scale = key_scale.reshape(heads_here, span_count, 1, KN * NTOK)
    value_blocks = values.reshape(heads_here, span_count, KN * NTOK, HD)
    scores = jnp.einsum("hcqd,hckd->hcqk", windows, key_blocks, preferred_element_type=jnp.float32)
    scores = scores * key_scale * (LOGIT_SCALE / math.sqrt(HD))
    expo = jnp.exp(scores)
    weights = (expo / jnp.sum(expo, axis=-1, keepdims=True)).astype(jnp.bfloat16)
    mixed = jnp.einsum("hcqk,hckd->cqhd", weights, value_blocks, preferred_element_type=jnp.float32)
    mixed = mixed.astype(jnp.bfloat16).reshape(seq_rows, heads_here * HD)
    leading = jnp.zeros((SPAN - 1, heads_here * HD), jnp.bfloat16)
    return jnp.concatenate([leading, mixed[: seq_rows - SPAN + 1]], axis=0)


def head_norm_major(projected):
    scaled = projected * lax.rsqrt(jnp.mean(projected * projected, axis=-1, keepdims=True) + EPSILON)
    return scaled.astype(jnp.bfloat16)

def ring_hops(states, n):
    to_right = [(i, (i + 1) % n) for i in range(n)]
    to_left = [(i, (i - 1) % n) for i in range(n)]
    going_right = states
    going_left = states
    right_hops = n // 2
    left_hops = n - 1 - right_hops
    steps = []
    for hop in range(1, right_hops + 1):
        step = {}
        going_right = lax.ppermute(going_right, "tensor", to_right)
        step[(n - hop) % n] = going_right
        if hop <= left_hops:
            going_left = lax.ppermute(going_left, "tensor", to_left)
            step[hop] = going_left
        steps.append(step)
    return steps


def ring_query(got, w_query, n):
    width = got[0].shape[1]
    me = lax.axis_index("tensor")
    total = None
    for offset in range(n):
        rows = lax.dynamic_slice_in_dim(w_query, ((me + offset) % n) * width, width, 0)
        term = jnp.dot(got[offset], rows, preferred_element_type=jnp.float32)
        total = term if total is None else total + term
    return total


def shards(hidden_states, neighbour_ids, database, w_up, w_down, w_query, w_key, w_value):
    dp_count = lax.axis_size("dp")
    tensor_count = lax.axis_size("tensor")
    shard_blocks = database.shape[0]
    block_tokens = database.shape[1]
    enc_width = database.shape[2]
    flat_ids = neighbour_ids.reshape(-1)
    request_count = flat_ids.shape[0]
    capacity = max(2, (request_count + dp_count - 1) // dp_count + 1)
    owners = flat_ids // shard_blocks
    local_rows = flat_ids % shard_blocks
    owner_match = (owners[:, None] == jnp.arange(dp_count, dtype=jnp.int32)[None, :]).astype(
        jnp.int32
    )
    positions = jnp.arange(request_count, dtype=jnp.int32)
    earlier = (positions[:, None] > positions[None, :]).astype(jnp.int32)
    ranks = jnp.sum(jnp.dot(earlier, owner_match) * owner_match, axis=1)
    slots = owners * capacity + ranks
    slot_match = slots[None, :] == jnp.arange(dp_count * capacity, dtype=jnp.int32)[:, None]
    requests = jnp.sum(jnp.where(slot_match, local_rows[None, :], 0), axis=1)
    requests = requests.reshape(dp_count, capacity)
    raw_float = database.astype(jnp.float32)
    normed = (
        raw_float * lax.rsqrt(jnp.mean(raw_float * raw_float, axis=-1, keepdims=True) + EPSILON)
    ).astype(jnp.bfloat16)
    inner = jnp.einsum("bte,ef->btf", normed, w_up, preferred_element_type=jnp.float32)
    active = jax.nn.gelu(inner).astype(jnp.bfloat16)
    partial = jnp.einsum("btf,fe->bte", active, w_down, preferred_element_type=jnp.float32)
    rows_here = block_tokens // tensor_count
    states = hidden_states[SPAN - 1 :]
    head_rows = SPAN
    head_got = {0: states[:head_rows]}
    for step in ring_hops(states[:head_rows], tensor_count):
        head_got.update(step)
    summed = lax.psum_scatter(
        partial.astype(jnp.bfloat16), "tensor", scatter_dimension=1, tiled=True
    )
    states_rest, summed = lax.optimization_barrier((states[head_rows:], summed))
    summed = summed.astype(jnp.float32)
    raw_own = lax.dynamic_slice_in_dim(
        raw_float, lax.axis_index("tensor") * rows_here, rows_here, 1
    )
    encoded_own = (raw_own + summed).astype(jnp.bfloat16)
    asked = lax.all_to_all(requests, "dp", split_axis=0, concat_axis=0, tiled=True)
    served, head_got = lax.optimization_barrier((encoded_own[asked], head_got))
    replies = lax.all_to_all(served, "dp", split_axis=0, concat_axis=0, tiled=True)
    mine = replies.reshape(dp_count * capacity, rows_here, enc_width)[slots]
    encoded = lax.all_gather(mine, "tensor", axis=1, tiled=True)
    heads_here = w_query.shape[1] // HD
    states_rest = lax.all_gather(states_rest, "tensor", axis=1, tiled=True)
    projected = jnp.concatenate(
        [
            ring_query(head_got, w_query, tensor_count),
            jnp.dot(states_rest, w_query, preferred_element_type=jnp.float32),
        ],
        axis=0,
    )
    queries = head_norm_major(projected.reshape(projected.shape[0], heads_here, HD))
    queries = jnp.transpose(queries, (1, 0, 2))
    flat_encoded = encoded.reshape(-1, enc_width)
    keys = jnp.einsum(
        "ke,ehd->hkd",
        flat_encoded,
        w_key.reshape(enc_width, heads_here, HD),
        preferred_element_type=jnp.float32,
    )
    key_scale = lax.rsqrt(jnp.mean(keys * keys, axis=-1) + EPSILON)
    keys = keys.astype(jnp.bfloat16)
    values = jnp.einsum(
        "ke,ehd->hkd",
        flat_encoded,
        w_value.reshape(enc_width, heads_here, HD),
        preferred_element_type=jnp.float32,
    ).astype(jnp.bfloat16)
    return attend(queries, keys, key_scale, values)

def solution(mesh):
    in_specs = (
        P("dp", "tensor"),
        P("dp", None),
        P("dp", None, None),
        P(None, "tensor"),
        P("tensor", None),
        P(None, "tensor"),
        P(None, "tensor"),
        P(None, "tensor"),
    )
    out_specs = P("dp", "tensor")
    return jax.shard_map(shards, mesh=mesh, in_specs=in_specs, out_specs=out_specs, check_vma=False)
```

```python
import math

import jax
import jax.numpy as jnp
from jax import lax
from jax.sharding import PartitionSpec as P

HD = 128
SPAN = 64
KN = 2
NTOK = 128


EPSILON = 1e-06
LOGIT_SCALE = 3.0


def head_norm(projected):
    shaped = projected.reshape(projected.shape[0], -1, HD)
    scaled = shaped * lax.rsqrt(jnp.mean(shaped * shaped, axis=-1, keepdims=True) + EPSILON)
    return scaled.astype(jnp.bfloat16)


def attend(queries, keys, values):
    heads_here = queries.shape[0]
    seq_rows = queries.shape[1] + SPAN - 1
    span_count = seq_rows // SPAN
    shifted = jnp.concatenate(
        [queries, jnp.zeros((heads_here, SPAN - 1, HD), jnp.bfloat16)], axis=1
    )
    windows = shifted.reshape(heads_here, span_count, SPAN, HD)
    key_blocks = keys.reshape(heads_here, span_count, KN * NTOK, HD)
    value_blocks = values.reshape(heads_here, span_count, KN * NTOK, HD)
    scores = jnp.einsum("hcqd,hckd->hcqk", windows, key_blocks, preferred_element_type=jnp.float32)
    scores = scores * (LOGIT_SCALE / math.sqrt(HD))
    expo = jnp.exp(scores)
    weights = (expo / jnp.sum(expo, axis=-1, keepdims=True)).astype(jnp.bfloat16)
    mixed = jnp.einsum("hcqk,hckd->cqhd", weights, value_blocks, preferred_element_type=jnp.float32)
    mixed = mixed.astype(jnp.bfloat16).reshape(seq_rows, heads_here * HD)
    leading = jnp.zeros((SPAN - 1, heads_here * HD), jnp.bfloat16)
    return jnp.concatenate([leading, mixed[: seq_rows - SPAN + 1]], axis=0)


def head_norm_major(projected):
    scaled = projected * lax.rsqrt(jnp.mean(projected * projected, axis=-1, keepdims=True) + EPSILON)
    return scaled.astype(jnp.bfloat16)

def ring_hops(states, n):
    to_right = [(i, (i + 1) % n) for i in range(n)]
    to_left = [(i, (i - 1) % n) for i in range(n)]
    going_right = states
    going_left = states
    right_hops = n // 2
    left_hops = n - 1 - right_hops
    steps = []
    for hop in range(1, right_hops + 1):
        step = {}
        going_right = lax.ppermute(going_right, "tensor", to_right)
        step[(n - hop) % n] = going_right
        if hop <= left_hops:
            going_left = lax.ppermute(going_left, "tensor", to_left)
            step[hop] = going_left
        steps.append(step)
    return steps


def ring_query(got, w_query, n):
    width = got[0].shape[1]
    me = lax.axis_index("tensor")
    total = None
    for offset in range(n):
        rows = lax.dynamic_slice_in_dim(w_query, ((me + offset) % n) * width, width, 0)
        term = jnp.dot(got[offset], rows, preferred_element_type=jnp.float32)
        total = term if total is None else total + term
    return total


def shards(hidden_states, neighbour_ids, database, w_up, w_down, w_query, w_key, w_value):
    dp_count = lax.axis_size("dp")
    tensor_count = lax.axis_size("tensor")
    shard_blocks = database.shape[0]
    block_tokens = database.shape[1]
    enc_width = database.shape[2]
    flat_ids = neighbour_ids.reshape(-1)
    request_count = flat_ids.shape[0]
    capacity = max(2, (request_count + dp_count - 1) // dp_count + 1)
    owners = flat_ids // shard_blocks
    local_rows = flat_ids % shard_blocks
    owner_match = (owners[:, None] == jnp.arange(dp_count, dtype=jnp.int32)[None, :]).astype(
        jnp.int32
    )
    positions = jnp.arange(request_count, dtype=jnp.int32)
    earlier = (positions[:, None] > positions[None, :]).astype(jnp.int32)
    ranks = jnp.sum(jnp.dot(earlier, owner_match) * owner_match, axis=1)
    slots = owners * capacity + ranks
    slot_match = slots[None, :] == jnp.arange(dp_count * capacity, dtype=jnp.int32)[:, None]
    requests = jnp.sum(jnp.where(slot_match, local_rows[None, :], 0), axis=1)
    requests = requests.reshape(dp_count, capacity)
    raw_float = database.astype(jnp.float32)
    normed = (
        raw_float * lax.rsqrt(jnp.mean(raw_float * raw_float, axis=-1, keepdims=True) + EPSILON)
    ).astype(jnp.bfloat16)
    inner = jnp.einsum("bte,ef->btf", normed, w_up, preferred_element_type=jnp.float32)
    active = jax.nn.gelu(inner).astype(jnp.bfloat16)
    partial = jnp.einsum("btf,fe->bte", active, w_down, preferred_element_type=jnp.float32)
    rows_here = block_tokens // tensor_count
    states = hidden_states[SPAN - 1 :]
    head_rows = SPAN
    head_got = {0: states[:head_rows]}
    for step in ring_hops(states[:head_rows], tensor_count):
        head_got.update(step)
    summed = lax.psum_scatter(
        partial.astype(jnp.bfloat16), "tensor", scatter_dimension=1, tiled=True
    )
    states_rest, summed, head_got = lax.optimization_barrier((states[head_rows:], summed, head_got))
    summed = summed.astype(jnp.float32)
    raw_own = lax.dynamic_slice_in_dim(
        raw_float, lax.axis_index("tensor") * rows_here, rows_here, 1
    )
    encoded_own = (raw_own + summed).astype(jnp.bfloat16)
    asked = lax.all_to_all(requests, "dp", split_axis=0, concat_axis=0, tiled=True)
    replies = lax.all_to_all(
        encoded_own[asked], "dp", split_axis=0, concat_axis=0, tiled=True
    )
    mine = replies.reshape(dp_count * capacity, rows_here, enc_width)[slots]
    encoded = lax.all_gather(mine, "tensor", axis=1, tiled=True)
    heads_here = w_query.shape[1] // HD
    states_rest = lax.all_gather(states_rest, "tensor", axis=1, tiled=True)
    projected = jnp.concatenate(
        [
            ring_query(head_got, w_query, tensor_count),
            jnp.dot(states_rest, w_query, preferred_element_type=jnp.float32),
        ],
        axis=0,
    )
    queries = head_norm_major(projected.reshape(projected.shape[0], heads_here, HD))
    queries = jnp.transpose(queries, (1, 0, 2))
    flat_encoded = encoded.reshape(-1, enc_width)
    keys = head_norm_major(
        jnp.einsum(
            "ke,ehd->hkd",
            flat_encoded,
            w_key.reshape(enc_width, heads_here, HD),
            preferred_element_type=jnp.float32,
        )
    )
    values = jnp.einsum(
        "ke,ehd->hkd",
        flat_encoded,
        w_value.reshape(enc_width, heads_here, HD),
        preferred_element_type=jnp.float32,
    ).astype(jnp.bfloat16)
    return attend(queries, keys, values)

def solution(mesh):
    in_specs = (
        P("dp", "tensor"),
        P("dp", None),
        P("dp", None, None),
        P(None, "tensor"),
        P("tensor", None),
        P(None, "tensor"),
        P(None, "tensor"),
        P(None, "tensor"),
    )
    out_specs = P("dp", "tensor")
    return jax.shard_map(shards, mesh=mesh, in_specs=in_specs, out_specs=out_specs, check_vma=False)
```

```python
import math

import jax
import jax.numpy as jnp
from jax import lax
from jax.sharding import PartitionSpec as P

HD = 128
SPAN = 64
KN = 2
NTOK = 128


EPSILON = 1e-06
LOGIT_SCALE = 3.0


def head_norm(projected):
    shaped = projected.reshape(projected.shape[0], -1, HD)
    scaled = shaped * lax.rsqrt(jnp.mean(shaped * shaped, axis=-1, keepdims=True) + EPSILON)
    return scaled.astype(jnp.bfloat16)


def attend(queries, keys, values):
    heads_here = queries.shape[0]
    seq_rows = queries.shape[1] + SPAN - 1
    span_count = seq_rows // SPAN
    shifted = jnp.concatenate(
        [queries, jnp.zeros((heads_here, SPAN - 1, HD), jnp.bfloat16)], axis=1
    )
    windows = shifted.reshape(heads_here, span_count, SPAN, HD)
    key_blocks = keys.reshape(heads_here, span_count, KN * NTOK, HD)
    value_blocks = values.reshape(heads_here, span_count, KN * NTOK, HD)
    scores = jnp.einsum("hcqd,hckd->hcqk", windows, key_blocks, preferred_element_type=jnp.float32)
    scores = scores * (LOGIT_SCALE / math.sqrt(HD))
    expo = jnp.exp(scores)
    weights = (expo / jnp.sum(expo, axis=-1, keepdims=True)).astype(jnp.bfloat16)
    mixed = jnp.einsum("hcqk,hckd->cqhd", weights, value_blocks, preferred_element_type=jnp.float32)
    mixed = mixed.astype(jnp.bfloat16).reshape(seq_rows, heads_here * HD)
    leading = jnp.zeros((SPAN - 1, heads_here * HD), jnp.bfloat16)
    return jnp.concatenate([leading, mixed[: seq_rows - SPAN + 1]], axis=0)


def head_norm_major(projected):
    scaled = projected * lax.rsqrt(jnp.mean(projected * projected, axis=-1, keepdims=True) + EPSILON)
    return scaled.astype(jnp.bfloat16)

def ring_hops(states, n):
    to_right = [(i, (i + 1) % n) for i in range(n)]
    to_left = [(i, (i - 1) % n) for i in range(n)]
    going_right = states
    going_left = states
    right_hops = n // 2
    left_hops = n - 1 - right_hops
    steps = []
    for hop in range(1, right_hops + 1):
        step = {}
        going_right = lax.ppermute(going_right, "tensor", to_right)
        step[(n - hop) % n] = going_right
        if hop <= left_hops:
            going_left = lax.ppermute(going_left, "tensor", to_left)
            step[hop] = going_left
        steps.append(step)
    return steps


def ring_query(got, w_query, n):
    width = got[0].shape[1]
    me = lax.axis_index("tensor")
    total = None
    for offset in range(n):
        rows = lax.dynamic_slice_in_dim(w_query, ((me + offset) % n) * width, width, 0)
        term = jnp.dot(got[offset], rows, preferred_element_type=jnp.float32)
        total = term if total is None else total + term
    return total


def shards(hidden_states, neighbour_ids, database, w_up, w_down, w_query, w_key, w_value):
    dp_count = lax.axis_size("dp")
    tensor_count = lax.axis_size("tensor")
    shard_blocks = database.shape[0]
    block_tokens = database.shape[1]
    enc_width = database.shape[2]
    flat_ids = neighbour_ids.reshape(-1)
    request_count = flat_ids.shape[0]
    capacity = max(2, (request_count + dp_count - 1) // dp_count + 1)
    owners = flat_ids // shard_blocks
    local_rows = flat_ids % shard_blocks
    owner_match = (owners[:, None] == jnp.arange(dp_count, dtype=jnp.int32)[None, :]).astype(
        jnp.int32
    )
    positions = jnp.arange(request_count, dtype=jnp.int32)
    earlier = (positions[:, None] > positions[None, :]).astype(jnp.int32)
    ranks = jnp.sum(jnp.dot(earlier, owner_match) * owner_match, axis=1)
    slots = owners * capacity + ranks
    slot_match = slots[None, :] == jnp.arange(dp_count * capacity, dtype=jnp.int32)[:, None]
    requests = jnp.sum(jnp.where(slot_match, local_rows[None, :], 0), axis=1)
    requests = requests.reshape(dp_count, capacity)
    raw_float = database.astype(jnp.float32)
    normed = (
        raw_float * lax.rsqrt(jnp.mean(raw_float * raw_float, axis=-1, keepdims=True) + EPSILON)
    ).astype(jnp.bfloat16)
    inner = jnp.einsum("bte,ef->btf", normed, w_up, preferred_element_type=jnp.float32)
    active = jax.nn.gelu(inner).astype(jnp.bfloat16)
    partial = jnp.einsum("btf,fe->bte", active, w_down, preferred_element_type=jnp.float32)
    rows_here = block_tokens // tensor_count
    states = hidden_states[SPAN - 1 :]
    head_rows = 2 * SPAN
    head_got = {0: states[:head_rows]}
    for step in ring_hops(states[:head_rows], tensor_count):
        head_got.update(step)
    summed = lax.psum_scatter(
        partial.astype(jnp.bfloat16), "tensor", scatter_dimension=1, tiled=True
    )
    states_rest, summed, head_got = lax.optimization_barrier((states[head_rows:], summed, head_got))
    summed = summed.astype(jnp.float32)
    raw_own = lax.dynamic_slice_in_dim(
        raw_float, lax.axis_index("tensor") * rows_here, rows_here, 1
    )
    encoded_own = (raw_own + summed).astype(jnp.bfloat16)
    asked = lax.all_to_all(requests, "dp", split_axis=0, concat_axis=0, tiled=True)
    replies = lax.all_to_all(
        encoded_own[asked], "dp", split_axis=0, concat_axis=0, tiled=True
    )
    mine = replies.reshape(dp_count * capacity, rows_here, enc_width)[slots]
    encoded = lax.all_gather(mine, "tensor", axis=1, tiled=True)
    heads_here = w_query.shape[1] // HD
    states_rest = lax.all_gather(states_rest, "tensor", axis=1, tiled=True)
    projected = jnp.concatenate(
        [
            ring_query(head_got, w_query, tensor_count),
            jnp.dot(states_rest, w_query, preferred_element_type=jnp.float32),
        ],
        axis=0,
    )
    queries = head_norm_major(projected.reshape(projected.shape[0], heads_here, HD))
    queries = jnp.transpose(queries, (1, 0, 2))
    flat_encoded = encoded.reshape(-1, enc_width)
    keys = head_norm_major(
        jnp.einsum(
            "ke,ehd->hkd",
            flat_encoded,
            w_key.reshape(enc_width, heads_here, HD),
            preferred_element_type=jnp.float32,
        )
    )
    values = jnp.einsum(
        "ke,ehd->hkd",
        flat_encoded,
        w_value.reshape(enc_width, heads_here, HD),
        preferred_element_type=jnp.float32,
    ).astype(jnp.bfloat16)
    return attend(queries, keys, values)

def solution(mesh):
    in_specs = (
        P("dp", "tensor"),
        P("dp", None),
        P("dp", None, None),
        P(None, "tensor"),
        P("tensor", None),
        P(None, "tensor"),
        P(None, "tensor"),
        P(None, "tensor"),
    )
    out_specs = P("dp", "tensor")
    return jax.shard_map(shards, mesh=mesh, in_specs=in_specs, out_specs=out_specs, check_vma=False)
```

```python
import math

import jax
import jax.numpy as jnp
from jax import lax
from jax.sharding import PartitionSpec as P

HD = 128
SPAN = 64
KN = 2
NTOK = 128


EPSILON = 1e-06
LOGIT_SCALE = 3.0


def head_norm(projected):
    shaped = projected.reshape(projected.shape[0], -1, HD)
    scaled = shaped * lax.rsqrt(jnp.mean(shaped * shaped, axis=-1, keepdims=True) + EPSILON)
    return scaled.astype(jnp.bfloat16)


def attend(queries, keys, values):
    heads_here = queries.shape[0]
    seq_rows = queries.shape[1] + SPAN - 1
    span_count = seq_rows // SPAN
    shifted = jnp.concatenate(
        [queries, jnp.zeros((heads_here, SPAN - 1, HD), jnp.bfloat16)], axis=1
    )
    windows = shifted.reshape(heads_here, span_count, SPAN, HD)
    key_blocks = keys.reshape(heads_here, span_count, KN * NTOK, HD)
    value_blocks = values.reshape(heads_here, span_count, KN * NTOK, HD)
    scores = jnp.einsum("hcqd,hckd->hcqk", windows, key_blocks, preferred_element_type=jnp.float32)
    scores = scores * (LOGIT_SCALE / math.sqrt(HD))
    expo = jnp.exp(scores)
    weights = (expo / jnp.sum(expo, axis=-1, keepdims=True)).astype(jnp.bfloat16)
    mixed = jnp.einsum("hcqk,hckd->cqhd", weights, value_blocks, preferred_element_type=jnp.float32)
    mixed = mixed.astype(jnp.bfloat16).reshape(seq_rows, heads_here * HD)
    leading = jnp.zeros((SPAN - 1, heads_here * HD), jnp.bfloat16)
    return jnp.concatenate([leading, mixed[: seq_rows - SPAN + 1]], axis=0)


def head_norm_major(projected):
    scaled = projected * lax.rsqrt(jnp.mean(projected * projected, axis=-1, keepdims=True) + EPSILON)
    return scaled.astype(jnp.bfloat16)

def ring_hops(states, n):
    to_right = [(i, (i + 1) % n) for i in range(n)]
    to_left = [(i, (i - 1) % n) for i in range(n)]
    going_right = states
    going_left = states
    right_hops = n // 2
    left_hops = n - 1 - right_hops
    steps = []
    for hop in range(1, right_hops + 1):
        step = {}
        going_right = lax.ppermute(going_right, "tensor", to_right)
        step[(n - hop) % n] = going_right
        if hop <= left_hops:
            going_left = lax.ppermute(going_left, "tensor", to_left)
            step[hop] = going_left
        steps.append(step)
    return steps


def ring_query(got, w_query, n):
    width = got[0].shape[1]
    me = lax.axis_index("tensor")
    total = None
    for offset in range(n):
        rows = lax.dynamic_slice_in_dim(w_query, ((me + offset) % n) * width, width, 0)
        term = jnp.dot(got[offset], rows, preferred_element_type=jnp.float32)
        total = term if total is None else total + term
    return total


def shards(hidden_states, neighbour_ids, database, w_up, w_down, w_query, w_key, w_value):
    dp_count = lax.axis_size("dp")
    tensor_count = lax.axis_size("tensor")
    shard_blocks = database.shape[0]
    block_tokens = database.shape[1]
    enc_width = database.shape[2]
    flat_ids = neighbour_ids.reshape(-1)
    request_count = flat_ids.shape[0]
    capacity = max(2, (request_count + dp_count - 1) // dp_count + 1)
    owners = flat_ids // shard_blocks
    local_rows = flat_ids % shard_blocks
    owner_match = (owners[:, None] == jnp.arange(dp_count, dtype=jnp.int32)[None, :]).astype(
        jnp.int32
    )
    positions = jnp.arange(request_count, dtype=jnp.int32)
    earlier = (positions[:, None] > positions[None, :]).astype(jnp.int32)
    ranks = jnp.sum(jnp.dot(earlier, owner_match) * owner_match, axis=1)
    slots = owners * capacity + ranks
    slot_match = slots[None, :] == jnp.arange(dp_count * capacity, dtype=jnp.int32)[:, None]
    requests = jnp.sum(jnp.where(slot_match, local_rows[None, :], 0), axis=1)
    requests = requests.reshape(dp_count, capacity)
    raw_float = database.astype(jnp.float32)
    normed = (
        raw_float * lax.rsqrt(jnp.mean(raw_float * raw_float, axis=-1, keepdims=True) + EPSILON)
    ).astype(jnp.bfloat16)
    inner = jnp.einsum("bte,ef->btf", normed, w_up, preferred_element_type=jnp.float32)
    active = jax.nn.gelu(inner).astype(jnp.bfloat16)
    partial = jnp.einsum("btf,fe->bte", active, w_down, preferred_element_type=jnp.float32)
    rows_here = block_tokens // tensor_count
    states = hidden_states[SPAN - 1 :]
    head_rows = 3 * SPAN
    head_got = {0: states[:head_rows]}
    for step in ring_hops(states[:head_rows], tensor_count):
        head_got.update(step)
    summed = lax.psum_scatter(
        partial.astype(jnp.bfloat16), "tensor", scatter_dimension=1, tiled=True
    )
    states_rest, summed, head_got = lax.optimization_barrier((states[head_rows:], summed, head_got))
    summed = summed.astype(jnp.float32)
    raw_own = lax.dynamic_slice_in_dim(
        raw_float, lax.axis_index("tensor") * rows_here, rows_here, 1
    )
    encoded_own = (raw_own + summed).astype(jnp.bfloat16)
    asked = lax.all_to_all(requests, "dp", split_axis=0, concat_axis=0, tiled=True)
    replies = lax.all_to_all(
        encoded_own[asked], "dp", split_axis=0, concat_axis=0, tiled=True
    )
    mine = replies.reshape(dp_count * capacity, rows_here, enc_width)[slots]
    encoded = lax.all_gather(mine, "tensor", axis=1, tiled=True)
    heads_here = w_query.shape[1] // HD
    states_rest = lax.all_gather(states_rest, "tensor", axis=1, tiled=True)
    projected = jnp.concatenate(
        [
            ring_query(head_got, w_query, tensor_count),
            jnp.dot(states_rest, w_query, preferred_element_type=jnp.float32),
        ],
        axis=0,
    )
    queries = head_norm_major(projected.reshape(projected.shape[0], heads_here, HD))
    queries = jnp.transpose(queries, (1, 0, 2))
    flat_encoded = encoded.reshape(-1, enc_width)
    keys = head_norm_major(
        jnp.einsum(
            "ke,ehd->hkd",
            flat_encoded,
            w_key.reshape(enc_width, heads_here, HD),
            preferred_element_type=jnp.float32,
        )
    )
    values = jnp.einsum(
        "ke,ehd->hkd",
        flat_encoded,
        w_value.reshape(enc_width, heads_here, HD),
        preferred_element_type=jnp.float32,
    ).astype(jnp.bfloat16)
    return attend(queries, keys, values)

def solution(mesh):
    in_specs = (
        P("dp", "tensor"),
        P("dp", None),
        P("dp", None, None),
        P(None, "tensor"),
        P("tensor", None),
        P(None, "tensor"),
        P(None, "tensor"),
        P(None, "tensor"),
    )
    out_specs = P("dp", "tensor")
    return jax.shard_map(shards, mesh=mesh, in_specs=in_specs, out_specs=out_specs, check_vma=False)
```

```python
import math

import jax
import jax.numpy as jnp
from jax import lax
from jax.sharding import PartitionSpec as P

HD = 128
SPAN = 64
KN = 2
NTOK = 128


EPSILON = 1e-06
LOGIT_SCALE = 3.0


def head_norm(projected):
    shaped = projected.reshape(projected.shape[0], -1, HD)
    scaled = shaped * lax.rsqrt(jnp.mean(shaped * shaped, axis=-1, keepdims=True) + EPSILON)
    return scaled.astype(jnp.bfloat16)


def attend(queries, keys, values):
    heads_here = queries.shape[0]
    seq_rows = queries.shape[1] + SPAN - 1
    span_count = seq_rows // SPAN
    shifted = jnp.concatenate(
        [queries, jnp.zeros((heads_here, SPAN - 1, HD), jnp.bfloat16)], axis=1
    )
    windows = shifted.reshape(heads_here, span_count, SPAN, HD)
    key_blocks = keys.reshape(heads_here, span_count, KN * NTOK, HD)
    value_blocks = values.reshape(heads_here, span_count, KN * NTOK, HD)
    scores = jnp.einsum("hcqd,hckd->hcqk", windows, key_blocks, preferred_element_type=jnp.float32)
    scores = scores * (LOGIT_SCALE / math.sqrt(HD))
    expo = jnp.exp(scores)
    weights = (expo / jnp.sum(expo, axis=-1, keepdims=True)).astype(jnp.bfloat16)
    mixed = jnp.einsum("hcqk,hckd->cqhd", weights, value_blocks, preferred_element_type=jnp.float32)
    mixed = mixed.astype(jnp.bfloat16).reshape(seq_rows, heads_here * HD)
    leading = jnp.zeros((SPAN - 1, heads_here * HD), jnp.bfloat16)
    return jnp.concatenate([leading, mixed[: seq_rows - SPAN + 1]], axis=0)


def head_norm_major(projected):
    scaled = projected * lax.rsqrt(jnp.mean(projected * projected, axis=-1, keepdims=True) + EPSILON)
    return scaled.astype(jnp.bfloat16)

def ring_hops(states, n):
    to_right = [(i, (i + 1) % n) for i in range(n)]
    to_left = [(i, (i - 1) % n) for i in range(n)]
    going_right = states
    going_left = states
    right_hops = n // 2
    left_hops = n - 1 - right_hops
    steps = []
    for hop in range(1, right_hops + 1):
        step = {}
        going_right = lax.ppermute(going_right, "tensor", to_right)
        step[(n - hop) % n] = going_right
        if hop <= left_hops:
            going_left = lax.ppermute(going_left, "tensor", to_left)
            step[hop] = going_left
        steps.append(step)
    return steps


def ring_query(got, w_query, n):
    width = got[0].shape[1]
    me = lax.axis_index("tensor")
    total = None
    for offset in range(n):
        rows = lax.dynamic_slice_in_dim(w_query, ((me + offset) % n) * width, width, 0)
        term = jnp.dot(got[offset], rows, preferred_element_type=jnp.float32)
        total = term if total is None else total + term
    return total


def shards(hidden_states, neighbour_ids, database, w_up, w_down, w_query, w_key, w_value):
    dp_count = lax.axis_size("dp")
    tensor_count = lax.axis_size("tensor")
    shard_blocks = database.shape[0]
    block_tokens = database.shape[1]
    enc_width = database.shape[2]
    flat_ids = neighbour_ids.reshape(-1)
    request_count = flat_ids.shape[0]
    capacity = max(2, (request_count + dp_count - 1) // dp_count + 1)
    owners = flat_ids // shard_blocks
    local_rows = flat_ids % shard_blocks
    owner_match = (owners[:, None] == jnp.arange(dp_count, dtype=jnp.int32)[None, :]).astype(
        jnp.int32
    )
    positions = jnp.arange(request_count, dtype=jnp.int32)
    earlier = (positions[:, None] > positions[None, :]).astype(jnp.int32)
    ranks = jnp.sum(jnp.dot(earlier, owner_match) * owner_match, axis=1)
    slots = owners * capacity + ranks
    slot_match = slots[None, :] == jnp.arange(dp_count * capacity, dtype=jnp.int32)[:, None]
    requests = jnp.sum(jnp.where(slot_match, local_rows[None, :], 0), axis=1)
    requests = requests.reshape(dp_count, capacity)
    raw_float = database.astype(jnp.float32)
    normed = (
        raw_float * lax.rsqrt(jnp.mean(raw_float * raw_float, axis=-1, keepdims=True) + EPSILON)
    ).astype(jnp.bfloat16)
    inner = jnp.einsum("bte,ef->btf", normed, w_up, preferred_element_type=jnp.float32)
    active = jax.nn.gelu(inner).astype(jnp.bfloat16)
    partial = jnp.einsum("btf,fe->bte", active, w_down, preferred_element_type=jnp.float32)
    rows_here = block_tokens // tensor_count
    states = hidden_states[SPAN - 1 :]
    head_rows = 4 * SPAN
    head_got = {0: states[:head_rows]}
    for step in ring_hops(states[:head_rows], tensor_count):
        head_got.update(step)
    summed = lax.psum_scatter(
        partial.astype(jnp.bfloat16), "tensor", scatter_dimension=1, tiled=True
    )
    states_rest, summed, head_got = lax.optimization_barrier((states[head_rows:], summed, head_got))
    summed = summed.astype(jnp.float32)
    raw_own = lax.dynamic_slice_in_dim(
        raw_float, lax.axis_index("tensor") * rows_here, rows_here, 1
    )
    encoded_own = (raw_own + summed).astype(jnp.bfloat16)
    asked = lax.all_to_all(requests, "dp", split_axis=0, concat_axis=0, tiled=True)
    replies = lax.all_to_all(
        encoded_own[asked], "dp", split_axis=0, concat_axis=0, tiled=True
    )
    mine = replies.reshape(dp_count * capacity, rows_here, enc_width)[slots]
    encoded = lax.all_gather(mine, "tensor", axis=1, tiled=True)
    heads_here = w_query.shape[1] // HD
    states_rest = lax.all_gather(states_rest, "tensor", axis=1, tiled=True)
    projected = jnp.concatenate(
        [
            ring_query(head_got, w_query, tensor_count),
            jnp.dot(states_rest, w_query, preferred_element_type=jnp.float32),
        ],
        axis=0,
    )
    queries = head_norm_major(projected.reshape(projected.shape[0], heads_here, HD))
    queries = jnp.transpose(queries, (1, 0, 2))
    flat_encoded = encoded.reshape(-1, enc_width)
    keys = head_norm_major(
        jnp.einsum(
            "ke,ehd->hkd",
            flat_encoded,
            w_key.reshape(enc_width, heads_here, HD),
            preferred_element_type=jnp.float32,
        )
    )
    values = jnp.einsum(
        "ke,ehd->hkd",
        flat_encoded,
        w_value.reshape(enc_width, heads_here, HD),
        preferred_element_type=jnp.float32,
    ).astype(jnp.bfloat16)
    return attend(queries, keys, values)

def solution(mesh):
    in_specs = (
        P("dp", "tensor"),
        P("dp", None),
        P("dp", None, None),
        P(None, "tensor"),
        P("tensor", None),
        P(None, "tensor"),
        P(None, "tensor"),
        P(None, "tensor"),
    )
    out_specs = P("dp", "tensor")
    return jax.shard_map(shards, mesh=mesh, in_specs=in_specs, out_specs=out_specs, check_vma=False)
```
